32 devices in a mesh: row: 16 (over z, y, x), col: 2 (over core).
Axes of the slice: x: 2, y: 2, z: 4, core: 2. Of those that a mesh axis runs over, the one named last changes fastest.
Arguments:
- air_state: bfloat16 [4096, 384], P(('row', 'col')), may hold values from -6 to 6
- owner_map: int32 [4096, 1], P(('row', 'col')), may hold values from 0 to 15; in each aligned block of 128 rows (0 to 127, 128 to 255, ...) at most 16 rows name the same one
- cost_class: int32 [4096], P(('row', 'col')), may hold values from 0 to 3
- connectivity: int32 [4, 4096], P(None, ('row', 'col')), may hold values from -32 to 32, as said below
- inverse_blocks: bfloat16 [32, 4, 3, 128, 128], P(('row', 'col')), may hold values from -0.5 to 0.5
Outputs:
- new_state: bfloat16 [4096, 384], P(('row', 'col'))
The draws below stay inside these ranges and needn't reach their ends.
Inputs may be any that keep to these rules, and one draw needn't show every extreme that they name: `owner_map`: among the columns of one device no owner row is named by more than 16 columns, and some owner row is named by exactly 16. `connectivity`: offsets are never zero; both ends of the range occur.
All inputs are finite; a program needn't handle non-finite values.
Results may differ from the reference program's by a relative error of at most 0.0037.
Values may be sent and summed in bfloat16 or wider, within the bound.
No kernel may reach another device: no remote copies, remote signals or barrier semaphores. Data moves between devices by JAX's collectives and lax.ppermute only.
A program may use at most 128 MiB of HBM per device.

```python
import math
import jax
import jax.numpy as jnp
import numpy as np
from jax import lax

LEV = 128
NCLASS = 4
PARTNERS = 4
COLS_DEV = 128
FEAT = 384
EDGE = 32
CAP = 16
GROUP_COLS = 256
OWNERS = 32
COLUMNS = 4096
N_ROW = 16
N_COL = 2


def draw_connectivity(key, part):
    size_key, sign_key = jax.random.split(key)
    magnitude = jax.random.randint(size_key, (PARTNERS, COLUMNS), 1, EDGE + 1)
    sign_draw = jax.random.randint(sign_key, (PARTNERS, COLUMNS), 0, 2) * 2 - 1
    offsets = (magnitude * sign_draw).astype(jnp.int32)
    return offsets.at[0, 0].set(EDGE).at[1, 0].set(-EDGE)


def set_ends(entries, own_key, least, top_value):
    index_at = [jax.random.randint(jax.random.fold_in(own_key, axis), (), 0, length) for axis, length in enumerate(entries.shape)]
    widest = entries.shape.index(max(entries.shape))
    next_to = index_at[:widest] + [(index_at[widest] + 1) % entries.shape[widest]] + index_at[widest + 1:]
    return entries.at[tuple(index_at)].set(least).at[tuple(next_to)].set(top_value)


def block_scale(key, dims, cuts, low, largest):
    gain = 1.0
    for dim, blocks in cuts:
        steps = jax.random.uniform(jax.random.fold_in(jax.random.fold_in(key, 6), dim), (blocks,), jnp.float32, low / len(cuts), largest / len(cuts))
        gain = gain * jnp.repeat(jnp.exp(steps), dims[dim] // blocks).reshape((-1,) + (1,) * (len(dims) - 1 - dim))
    return gain


def shared_out(own_key, own, number, rows, count, top, limit, lean):
    ranking = jax.random.permutation(own_key, count)
    crowded, common = portions_of(count, rows * top, limit, lean, True), portions_of(count, rows * top, limit, lean, False)
    places = jnp.arange(count)

    def named(lengths, rotation):
        used = int((lengths > 0).sum())
        fixed = max(1, used // 4)
        passed = fixed + (places - fixed + rotation * (used - fixed)) % max(1, count - fixed)
        return jnp.zeros((count,), jnp.int32).at[ranking[jnp.where(places < fixed, places, passed)]].set(jnp.asarray(lengths, jnp.int32))

    lengths = jnp.where(number % 4 == 0, named(crowded, number // 4), named(common, number - number // 4 - 1))
    mixed = jax.random.permutation(jax.random.fold_in(own, 3), count)
    donor, sink = mixed[0:count // 2 * 2:2], mixed[1:count // 2 * 2:2]
    slack = jnp.minimum(lengths[donor] - 1, limit - lengths[sink]) // 2
    slack = jnp.where((donor == ranking[0]) | (sink == ranking[0]) | (lengths[sink] == 0), 0, jnp.maximum(slack, 0))
    passed = jax.random.randint(jax.random.fold_in(own, 4), (count // 2,), 0, 1 << 20) % (slack + 1)
    lengths = lengths.at[donor].add(-passed).at[sink].add(passed)
    items = jnp.searchsorted(jnp.cumsum(lengths), jnp.arange(rows * top), side="right").astype(jnp.int32)
    listing = items.reshape(top, rows).T
    listing = listing[jax.random.permutation(jax.random.fold_in(own, 1), rows)]
    rotation = jax.random.randint(jax.random.fold_in(own, 2), (rows, 1), 0, top)
    return jnp.take_along_axis(listing, (jnp.arange(top)[None, :] + rotation) % top, axis=1)


def portions_of(count, total, reach, lean, full):
    weights = [(1 << 20) // math.isqrt(grade ** lean) + 1 for grade in range(1, count + 1)]
    largest = reach if full else min(reach, max(-(-total // count), total * weights[0] // sum(weights)))
    least = 1 if total - largest >= count - 1 else 0
    given, surplus = [largest] + [least] * (count - 1), total - largest - least * (count - 1)
    while surplus > 0:
        free = [i for i in range(1, count) if given[i] < largest] or [i for i in range(1, count) if given[i] < reach]
        mass, left = sum([weights[i] for i in free]), surplus
        for i in free:
            addition = min(reach - given[i], max(1, left * weights[i] // mass), surplus)
            given[i] = given[i] + addition
            surplus = surplus - addition
    return np.array(given)


def gaussian(stream_key, shape, width, bound, pieces=(), held_as=jnp.bfloat16):
    loudness = block_scale(stream_key, shape, pieces, -0.22, 0.18) if pieces else 1.0
    entries = jax.random.normal(stream_key, shape, jnp.float32) * width * loudness
    return jnp.minimum(jnp.maximum(entries, -bound), bound).astype(held_as)


def setup_inputs(seed: int = 0) -> dict:
    arg_keys = jax.random.split(jax.random.key(seed), 6)
    air_state = gaussian(arg_keys[0], (COLUMNS, FEAT), 1.0, 6.0, ((0, 32),))
    owner_map_keys = jax.random.split(jax.random.fold_in(arg_keys[1], 1), COLUMNS // COLS_DEV)
    owner_map_turns = jax.random.permutation(jax.random.fold_in(arg_keys[1], 3), COLUMNS // COLS_DEV)
    owner_map = jax.vmap(lambda own, number: shared_out(jax.random.fold_in(arg_keys[1], 2), own, number, COLS_DEV, N_ROW, 1, CAP, 2))(owner_map_keys, owner_map_turns).reshape((COLUMNS, 1))
    cost_class = set_ends(jax.random.randint(arg_keys[2], (COLUMNS,), 0, NCLASS), jax.random.fold_in(arg_keys[2], 1), 0, NCLASS - 1).astype(jnp.int32)
    connectivity = draw_connectivity(jax.random.fold_in(arg_keys[5], 71), 0)
    inverse_blocks = gaussian(arg_keys[4], (OWNERS, NCLASS, 3, LEV, LEV), LEV ** -0.5, 0.5, ((0, 32),))
    return dict(air_state=air_state, owner_map=owner_map, cost_class=cost_class, connectivity=connectivity, inverse_blocks=inverse_blocks)


viscosity = 0.25


def apply_blocks(air_state, owner_map, cost_class, inverse_blocks):
    column_total = air_state.shape[0]
    position = jnp.arange(column_total, dtype=jnp.int32)
    owners = owner_map[:, 0] * N_COL + (position // COLS_DEV) % N_COL
    op_index = (owners * NCLASS + cost_class).astype(jnp.int32)
    all_blocks = inverse_blocks.reshape(OWNERS * NCLASS, 3, LEV, LEV)
    block_size = min(256, COLS_DEV)
    block_count = column_total // block_size

    def one_block(pair):
        row_block, block_picks = pair
        blocks = all_blocks[block_picks].astype(jnp.float32)
        fields = row_block.reshape(block_size, 3, LEV).astype(jnp.float32)
        result = jnp.einsum("nfm,nflm->nfl", fields, blocks)
        return result.reshape(block_size, FEAT).astype(jnp.bfloat16)

    physics = lax.map(one_block, (air_state.reshape(block_count, block_size, FEAT), op_index.reshape(block_count, block_size)))
    return physics.reshape(column_total, FEAT)


def edge_sums(air_state, connectivity):
    grouped = air_state.astype(jnp.float32).reshape(N_ROW, GROUP_COLS, FEAT)
    offsets = connectivity.reshape(PARTNERS, N_ROW, GROUP_COLS)
    places = jnp.arange(GROUP_COLS, dtype=jnp.int32)[None, :]
    laplace_sum = jnp.zeros_like(grouped)
    for partner in range(PARTNERS):
        target = ((places + offsets[partner]) % GROUP_COLS).astype(jnp.int32)
        gathered = jax.vmap(lambda source_table, row_picks: source_table[row_picks])(grouped, target)
        laplace_sum = laplace_sum + (gathered - grouped)
    return laplace_sum.reshape(N_ROW * GROUP_COLS, FEAT)


def reference(air_state, owner_map, cost_class, connectivity, inverse_blocks):
    physics = apply_blocks(air_state, owner_map, cost_class, inverse_blocks)
    laplace_sum = edge_sums(air_state, connectivity)
    return (physics.astype(jnp.float32) + viscosity * laplace_sum).astype(jnp.bfloat16)
```

```python
import jax
import jax.numpy as jnp
from jax import lax
from jax.sharding import PartitionSpec as P

viscosity = 0.25


def padded(cells, axis, width):
    count = lax.axis_size(axis)
    head = cells[:width]
    tail = cells[cells.shape[0] - width:]
    return jnp.concatenate(
        [
            lax.ppermute(tail, axis, [(i, (i + 1) % count) for i in range(count)]),
            cells,
            lax.ppermute(head, axis, [((i + 1) % count, i) for i in range(count)]),
        ],
        axis=0,
    )


def per_device(air_state, owner_map, cost_class, connectivity, inverse_blocks):
    groups = lax.axis_size("row")
    local_count, feat = air_state.shape
    levels = inverse_blocks.shape[-1]
    classes = inverse_blocks.shape[1]
    fields = feat // levels
    capacity = 2 * local_count // groups
    slots = groups * capacity

    targets = owner_map[:, 0]
    hits = (targets[:, None] == jnp.arange(groups, dtype=jnp.int32)[None, :]).astype(jnp.int32)
    slot_index = jnp.sum((jnp.cumsum(hits, axis=0) - 1) * hits, axis=1)
    dest = targets * capacity + slot_index
    pack = (jnp.arange(slots, dtype=jnp.int32)[:, None] == dest[None, :]).astype(jnp.bfloat16)

    label_lanes = jnp.broadcast_to(cost_class.astype(jnp.bfloat16)[:, None], (local_count, 128))
    air_ext = jnp.concatenate([air_state, label_lanes], axis=1)
    outgoing = jnp.dot(pack, air_ext, preferred_element_type=jnp.float32).astype(jnp.bfloat16)
    received = lax.all_to_all(
        outgoing.reshape(groups, capacity, feat + 128), "row", split_axis=0, concat_axis=0, tiled=True
    ).reshape(slots, feat + 128)

    halo = local_count // 4
    extended = padded(air_state, "col", halo)
    base = jnp.arange(local_count, dtype=jnp.int32)[:, None] + halo
    cols = jnp.arange(local_count + 2 * halo, dtype=jnp.int32)[None, :]
    counts = jnp.zeros((local_count, local_count + 2 * halo), jnp.float32)
    for partner in range(connectivity.shape[0]):
        counts = counts + (cols == base + connectivity[partner][:, None]).astype(jnp.float32)
    counts = counts - connectivity.shape[0] * (cols == base).astype(jnp.float32)
    band = (viscosity * counts).astype(jnp.bfloat16)
    lap = jnp.dot(band, extended, preferred_element_type=jnp.float32)

    labels = received[:, feat:feat + 1]
    own_blocks = inverse_blocks[0]
    outs = []
    for f in range(fields):
        xf = received[:, f * levels:(f + 1) * levels]
        acc = jnp.zeros((slots, levels), jnp.float32)
        for c in range(classes):
            r = lax.dot_general(
                xf, own_blocks[c, f], (((1,), (1,)), ((), ())), preferred_element_type=jnp.float32
            )
            acc = jnp.where(labels == c, r, acc)
        outs.append(acc.astype(jnp.bfloat16))
    computed = jnp.concatenate(outs, axis=1)
    returned = lax.all_to_all(
        computed.reshape(groups, capacity, feat), "row", split_axis=0, concat_axis=0, tiled=True
    ).reshape(slots, feat)
    physics = lax.dot_general(
        pack, returned, (((0,), (0,)), ((), ())), preferred_element_type=jnp.float32
    )
    return (physics + lap).astype(jnp.bfloat16)


def solution(mesh):
    return jax.shard_map(
        per_device,
        mesh=mesh,
        in_specs=(
            P(("row", "col"), None),
            P(("row", "col"), None),
            P(("row", "col")),
            P(None, ("row", "col")),
            P(("row", "col"), None, None, None, None),
        ),
        out_specs=P(("row", "col"), None),
        check_vma=False,
    )
```

```python
import jax
import jax.numpy as jnp
from jax import lax
from jax.experimental import pallas as pl
from jax.experimental.pallas import tpu as pltpu
from jax.sharding import PartitionSpec as P

viscosity = 0.25


def padded(cells, axis, width):
    count = lax.axis_size(axis)
    head = cells[:width]
    tail = cells[cells.shape[0] - width:]
    return jnp.concatenate(
        [
            lax.ppermute(tail, axis, [(i, (i + 1) % count) for i in range(count)]),
            cells,
            lax.ppermute(head, axis, [((i + 1) % count, i) for i in range(count)]),
        ],
        axis=0,
    )


def owner_kernel(x_ref, m_ref, o_ref):
    classes, fields, levels = m_ref.shape[0], m_ref.shape[1], m_ref.shape[2]
    feat = fields * levels
    labels = x_ref[:, feat:feat + 1].astype(jnp.float32)
    for f in range(fields):
        xf = x_ref[:, f * levels:(f + 1) * levels]
        acc = None
        for c in range(classes):
            r = lax.dot_general(
                xf, m_ref[c, f], (((1,), (1,)), ((), ())), preferred_element_type=jnp.float32
            )
            acc = r if acc is None else jnp.where(labels == c, r, acc)
        o_ref[:, f * levels:(f + 1) * levels] = acc.astype(o_ref.dtype)


def apply_owner(received, own_blocks):
    slots = received.shape[0]
    classes, fields, levels = own_blocks.shape[0], own_blocks.shape[1], own_blocks.shape[2]
    return pl.pallas_call(
        owner_kernel,
        out_shape=jax.ShapeDtypeStruct((slots, fields * levels), jnp.bfloat16),
        in_specs=[pl.BlockSpec(memory_space=pltpu.VMEM)] * 2,
        out_specs=pl.BlockSpec(memory_space=pltpu.VMEM),
        cost_estimate=pl.CostEstimate(
            flops=2 * slots * classes * fields * levels * levels,
            transcendentals=0,
            bytes_accessed=2 * (received.size + own_blocks.size + slots * fields * levels),
        ),
    )(received, own_blocks)


def per_device(air_state, owner_map, cost_class, connectivity, inverse_blocks):
    groups = lax.axis_size("row")
    local_count, feat = air_state.shape
    levels = inverse_blocks.shape[-1]
    classes = inverse_blocks.shape[1]
    fields = feat // levels
    capacity = 2 * local_count // groups
    slots = groups * capacity

    targets = owner_map[:, 0]
    hits = (targets[:, None] == jnp.arange(groups, dtype=jnp.int32)[None, :]).astype(jnp.int32)
    slot_index = jnp.sum((jnp.cumsum(hits, axis=0) - 1) * hits, axis=1)
    dest = targets * capacity + slot_index
    pack = (jnp.arange(slots, dtype=jnp.int32)[:, None] == dest[None, :]).astype(jnp.bfloat16)

    label_lanes = jnp.broadcast_to(cost_class.astype(jnp.bfloat16)[:, None], (local_count, 128))
    air_ext = jnp.concatenate([air_state, label_lanes], axis=1)
    outgoing = jnp.dot(pack, air_ext, preferred_element_type=jnp.float32).astype(jnp.bfloat16)
    received = lax.all_to_all(
        outgoing.reshape(groups, capacity, feat + 128), "row", split_axis=0, concat_axis=0, tiled=True
    ).reshape(slots, feat + 128)

    halo = local_count // 4
    extended = padded(air_state, "col", halo)
    base = jnp.arange(local_count, dtype=jnp.int32)[:, None] + halo
    cols = jnp.arange(local_count + 2 * halo, dtype=jnp.int32)[None, :]
    counts = jnp.zeros((local_count, local_count + 2 * halo), jnp.float32)
    for partner in range(connectivity.shape[0]):
        counts = counts + (cols == base + connectivity[partner][:, None]).astype(jnp.float32)
    counts = counts - connectivity.shape[0] * (cols == base).astype(jnp.float32)
    band = (viscosity * counts).astype(jnp.bfloat16)
    lap = jnp.dot(band, extended, preferred_element_type=jnp.float32)

    computed = apply_owner(received, inverse_blocks[0])
    returned = lax.all_to_all(
        computed.reshape(groups, capacity, feat), "row", split_axis=0, concat_axis=0, tiled=True
    ).reshape(slots, feat)
    physics = lax.dot_general(
        pack, returned, (((0,), (0,)), ((), ())), preferred_element_type=jnp.float32
    )
    return (physics + lap).astype(jnp.bfloat16)


def solution(mesh):
    return jax.shard_map(
        per_device,
        mesh=mesh,
        in_specs=(
            P(("row", "col"), None),
            P(("row", "col"), None),
            P(("row", "col")),
            P(None, ("row", "col")),
            P(("row", "col"), None, None, None, None),
        ),
        out_specs=P(("row", "col"), None),
        check_vma=False,
    )
```

```python
import jax
import jax.numpy as jnp
from jax import lax
from jax.experimental import pallas as pl
from jax.experimental.pallas import tpu as pltpu
from jax.sharding import PartitionSpec as P

viscosity = 0.25


def padded(cells, axis, width):
    count = lax.axis_size(axis)
    head = cells[:width]
    tail = cells[cells.shape[0] - width:]
    return jnp.concatenate(
        [
            lax.ppermute(tail, axis, [(i, (i + 1) % count) for i in range(count)]),
            cells,
            lax.ppermute(head, axis, [((i + 1) % count, i) for i in range(count)]),
        ],
        axis=0,
    )


def owner_kernel(x_hbm, m_hbm, o_hbm, xbuf, mbuf, obuf, sems):
    classes, fields, levels = mbuf.shape[0], mbuf.shape[1], mbuf.shape[2]
    feat = fields * levels
    fetch_x = pltpu.make_async_copy(x_hbm, xbuf, sems.at[0])
    fetch_x.start()
    fetch_m = [
        pltpu.make_async_copy(m_hbm.at[:, f], mbuf.at[:, f], sems.at[1 + f]) for f in range(fields)
    ]
    for copy in fetch_m:
        copy.start()
    fetch_x.wait()
    labels = xbuf[:, feat:feat + 1].astype(jnp.float32)
    stores = []
    for f in range(fields):
        fetch_m[f].wait()
        xf = xbuf[:, f * levels:(f + 1) * levels]
        stacked = mbuf[:, f].reshape(classes * levels, levels)
        r = lax.dot_general(xf, stacked, (((1,), (1,)), ((), ())), preferred_element_type=jnp.float32)
        acc = r[:, :levels]
        for c in range(1, classes):
            acc = jnp.where(labels == c, r[:, c * levels:(c + 1) * levels], acc)
        obuf[:, f * levels:(f + 1) * levels] = acc.astype(obuf.dtype)
        store = pltpu.make_async_copy(
            obuf.at[:, pl.ds(f * levels, levels)],
            o_hbm.at[:, pl.ds(f * levels, levels)],
            sems.at[1 + fields + f],
        )
        store.start()
        stores.append(store)
    for store in stores:
        store.wait()


def apply_owner(received, own_blocks):
    slots = received.shape[0]
    classes, fields, levels = own_blocks.shape[0], own_blocks.shape[1], own_blocks.shape[2]
    return pl.pallas_call(
        owner_kernel,
        out_shape=jax.ShapeDtypeStruct((slots, fields * levels), jnp.bfloat16),
        in_specs=[pl.BlockSpec(memory_space=pl.ANY)] * 2,
        out_specs=pl.BlockSpec(memory_space=pl.ANY),
        scratch_shapes=[
            pltpu.VMEM(received.shape, received.dtype),
            pltpu.VMEM(own_blocks.shape, own_blocks.dtype),
            pltpu.VMEM((slots, fields * levels), jnp.bfloat16),
            pltpu.SemaphoreType.DMA((1 + 2 * fields,)),
        ],
        cost_estimate=pl.CostEstimate(
            flops=2 * slots * classes * fields * levels * levels,
            transcendentals=0,
            bytes_accessed=2 * (received.size + own_blocks.size + slots * fields * levels),
        ),
    )(received, own_blocks)


def per_device(air_state, owner_map, cost_class, connectivity, inverse_blocks):
    groups = lax.axis_size("row")
    local_count, feat = air_state.shape
    levels = inverse_blocks.shape[-1]
    classes = inverse_blocks.shape[1]
    fields = feat // levels
    capacity = 2 * local_count // groups
    slots = groups * capacity

    targets = owner_map[:, 0]
    hits = (targets[:, None] == jnp.arange(groups, dtype=jnp.int32)[None, :]).astype(jnp.int32)
    slot_index = jnp.sum((jnp.cumsum(hits, axis=0) - 1) * hits, axis=1)
    dest = targets * capacity + slot_index
    pack = (jnp.arange(slots, dtype=jnp.int32)[:, None] == dest[None, :]).astype(jnp.bfloat16)

    label_lanes = jnp.broadcast_to(cost_class.astype(jnp.bfloat16)[:, None], (local_count, 128))
    air_ext = jnp.concatenate([air_state, label_lanes], axis=1)
    outgoing = jnp.dot(pack, air_ext, preferred_element_type=jnp.float32).astype(jnp.bfloat16)
    received = lax.all_to_all(
        outgoing.reshape(groups, capacity, feat + 128), "row", split_axis=0, concat_axis=0, tiled=True
    ).reshape(slots, feat + 128)

    halo = local_count // 4
    extended = padded(air_state, "col", halo)
    base = jnp.arange(local_count, dtype=jnp.int32)[:, None] + halo
    cols = jnp.arange(local_count + 2 * halo, dtype=jnp.int32)[None, :]
    counts = jnp.zeros((local_count, local_count + 2 * halo), jnp.float32)
    for partner in range(connectivity.shape[0]):
        counts = counts + (cols == base + connectivity[partner][:, None]).astype(jnp.float32)
    counts = counts - connectivity.shape[0] * (cols == base).astype(jnp.float32)
    band = (viscosity * counts).astype(jnp.bfloat16)
    lap = jnp.dot(band, extended, preferred_element_type=jnp.float32)

    received, lap = lax.optimization_barrier((received, lap))
    computed = apply_owner(received, inverse_blocks[0])
    returned = lax.all_to_all(
        computed.reshape(groups, capacity, feat), "row", split_axis=0, concat_axis=0, tiled=True
    ).reshape(slots, feat)
    physics = lax.dot_general(
        pack, returned, (((0,), (0,)), ((), ())), preferred_element_type=jnp.float32
    )
    return (physics + lap).astype(jnp.bfloat16)


def solution(mesh):
    return jax.shard_map(
        per_device,
        mesh=mesh,
        in_specs=(
            P(("row", "col"), None),
            P(("row", "col"), None),
            P(("row", "col")),
            P(None, ("row", "col")),
            P(("row", "col"), None, None, None, None),
        ),
        out_specs=P(("row", "col"), None),
        check_vma=False,
    )
```

```python
import jax
import jax.numpy as jnp
from jax import lax
from jax.experimental import pallas as pl
from jax.experimental.pallas import tpu as pltpu
from jax.sharding import PartitionSpec as P

viscosity = 0.25


def padded(cells, axis, width):
    count = lax.axis_size(axis)
    head = cells[:width]
    tail = cells[cells.shape[0] - width:]
    return jnp.concatenate(
        [
            lax.ppermute(tail, axis, [(i, (i + 1) % count) for i in range(count)]),
            cells,
            lax.ppermute(head, axis, [((i + 1) % count, i) for i in range(count)]),
        ],
        axis=0,
    )


def owner_kernel(x_ref, m_ref, o_ref):
    classes, fields, levels = m_ref.shape[0], m_ref.shape[1], m_ref.shape[2]
    feat = fields * levels
    labels = x_ref[:, feat:feat + 1].astype(jnp.float32)
    for f in range(fields):
        xf = x_ref[:, f * levels:(f + 1) * levels]
        acc = None
        for c in range(classes):
            r = lax.dot_general(
                xf, m_ref[c, f], (((1,), (1,)), ((), ())), preferred_element_type=jnp.float32
            )
            acc = r if acc is None else jnp.where(labels == c, r, acc)
        o_ref[:, f * levels:(f + 1) * levels] = acc.astype(o_ref.dtype)


def apply_owner(received, own_blocks):
    slots = received.shape[0]
    classes, fields, levels = own_blocks.shape[0], own_blocks.shape[1], own_blocks.shape[2]
    return pl.pallas_call(
        owner_kernel,
        out_shape=jax.ShapeDtypeStruct((slots, fields * levels), jnp.bfloat16),
        in_specs=[pl.BlockSpec(memory_space=pltpu.VMEM)] * 2,
        out_specs=pl.BlockSpec(memory_space=pltpu.VMEM),
        cost_estimate=pl.CostEstimate(
            flops=2 * slots * classes * fields * levels * levels,
            transcendentals=0,
            bytes_accessed=2 * (received.size + own_blocks.size + slots * fields * levels),
        ),
    )(
        pltpu.with_memory_space_constraint(received, pltpu.MemorySpace.VMEM),
        pltpu.with_memory_space_constraint(own_blocks, pltpu.MemorySpace.VMEM),
    )


def per_device(air_state, owner_map, cost_class, connectivity, inverse_blocks):
    groups = lax.axis_size("row")
    local_count, feat = air_state.shape
    levels = inverse_blocks.shape[-1]
    classes = inverse_blocks.shape[1]
    fields = feat // levels
    capacity = 2 * local_count // groups
    slots = groups * capacity

    targets = owner_map[:, 0]
    hits = (targets[:, None] == jnp.arange(groups, dtype=jnp.int32)[None, :]).astype(jnp.int32)
    slot_index = jnp.sum((jnp.cumsum(hits, axis=0) - 1) * hits, axis=1)
    dest = targets * capacity + slot_index
    pack = (jnp.arange(slots, dtype=jnp.int32)[:, None] == dest[None, :]).astype(jnp.bfloat16)

    label_lanes = jnp.broadcast_to(cost_class.astype(jnp.bfloat16)[:, None], (local_count, 128))
    air_ext = jnp.concatenate([air_state, label_lanes], axis=1)
    outgoing = jnp.dot(pack, air_ext, preferred_element_type=jnp.float32).astype(jnp.bfloat16)
    received = lax.all_to_all(
        outgoing.reshape(groups, capacity, feat + 128), "row", split_axis=0, concat_axis=0, tiled=True
    ).reshape(slots, feat + 128)

    halo = local_count // 4
    extended = padded(air_state, "col", halo)
    base = jnp.arange(local_count, dtype=jnp.int32)[:, None] + halo
    cols = jnp.arange(local_count + 2 * halo, dtype=jnp.int32)[None, :]
    counts = jnp.zeros((local_count, local_count + 2 * halo), jnp.float32)
    for partner in range(connectivity.shape[0]):
        counts = counts + (cols == base + connectivity[partner][:, None]).astype(jnp.float32)
    counts = counts - connectivity.shape[0] * (cols == base).astype(jnp.float32)
    band = (viscosity * counts).astype(jnp.bfloat16)
    lap = jnp.dot(band, extended, preferred_element_type=jnp.float32)

    computed = apply_owner(received, inverse_blocks[0])
    returned = lax.all_to_all(
        computed.reshape(groups, capacity, feat), "row", split_axis=0, concat_axis=0, tiled=True
    ).reshape(slots, feat)
    physics = lax.dot_general(
        pack, returned, (((0,), (0,)), ((), ())), preferred_element_type=jnp.float32
    )
    return (physics + lap).astype(jnp.bfloat16)


def solution(mesh):
    return jax.shard_map(
        per_device,
        mesh=mesh,
        in_specs=(
            P(("row", "col"), None),
            P(("row", "col"), None),
            P(("row", "col")),
            P(None, ("row", "col")),
            P(("row", "col"), None, None, None, None),
        ),
        out_specs=P(("row", "col"), None),
        check_vma=False,
    )
```

```python
import functools

import jax
import jax.numpy as jnp
from jax import lax
from jax.experimental import pallas as pl
from jax.experimental.pallas import tpu as pltpu
from jax.sharding import PartitionSpec as P

viscosity = 0.25


def padded(cells, axis, width):
    count = lax.axis_size(axis)
    head = cells[:width]
    tail = cells[cells.shape[0] - width:]
    return jnp.concatenate(
        [
            lax.ppermute(tail, axis, [(i, (i + 1) % count) for i in range(count)]),
            cells,
            lax.ppermute(head, axis, [((i + 1) % count, i) for i in range(count)]),
        ],
        axis=0,
    )


def pack_kernel(capacity, air_ref, owner_ref, class_ref, out_ref, dest_ref):
    count, feat = air_ref.shape
    slots = out_ref.shape[0]
    groups = slots // capacity
    owner = owner_ref[...]
    hits = (lax.broadcasted_iota(jnp.int32, (groups, count), 0) == owner).astype(jnp.float32)
    earlier = (
        lax.broadcasted_iota(jnp.int32, (count, count), 0)
        <= lax.broadcasted_iota(jnp.int32, (count, count), 1)
    ).astype(jnp.bfloat16)
    running = jnp.dot(hits.astype(jnp.bfloat16), earlier, preferred_element_type=jnp.float32)
    rank = jnp.sum(running * hits, axis=0, keepdims=True) - 1.0
    dest = owner * capacity + rank.astype(jnp.int32)
    dest_ref[...] = dest
    chosen = lax.broadcasted_iota(jnp.int32, (slots, count), 0) == dest
    moved = jnp.dot(chosen.astype(jnp.bfloat16), air_ref[...], preferred_element_type=jnp.float32)
    label = jnp.sum(jnp.where(chosen, class_ref[...].astype(jnp.float32), 0.0), axis=1, keepdims=True)
    out_ref[:, :feat] = moved.astype(out_ref.dtype)
    out_ref[:, feat:] = jnp.broadcast_to(label, (slots, out_ref.shape[1] - feat)).astype(out_ref.dtype)


def pack_columns(air_state, owner_row, class_row, capacity, slots):
    count, feat = air_state.shape
    vmem = pltpu.MemorySpace.VMEM
    return pl.pallas_call(
        functools.partial(pack_kernel, capacity),
        out_shape=(
            jax.ShapeDtypeStruct((slots, feat + 128), jnp.bfloat16),
            jax.ShapeDtypeStruct((1, count), jnp.int32),
        ),
        in_specs=[pl.BlockSpec(memory_space=pltpu.VMEM)] * 3,
        out_specs=(pl.BlockSpec(memory_space=pltpu.VMEM), pl.BlockSpec(memory_space=pltpu.VMEM)),
        cost_estimate=pl.CostEstimate(
            flops=2 * slots * count * feat + 2 * count * count * slots // capacity,
            transcendentals=0,
            bytes_accessed=2 * (air_state.size + slots * (feat + 128)) + 12 * count,
        ),
    )(
        pltpu.with_memory_space_constraint(air_state, vmem),
        pltpu.with_memory_space_constraint(owner_row, vmem),
        pltpu.with_memory_space_constraint(class_row, vmem),
    )


def owner_kernel(x_ref, m_ref, o_ref):
    classes, fields, levels = m_ref.shape[0], m_ref.shape[1], m_ref.shape[2]
    feat = fields * levels
    labels = x_ref[:, feat:feat + 1].astype(jnp.float32)
    for f in range(fields):
        xf = x_ref[:, f * levels:(f + 1) * levels]
        acc = None
        for c in range(classes):
            r = lax.dot_general(
                xf, m_ref[c, f], (((1,), (1,)), ((), ())), preferred_element_type=jnp.float32
            )
            acc = r if acc is None else jnp.where(labels == c, r, acc)
        o_ref[:, f * levels:(f + 1) * levels] = acc.astype(o_ref.dtype)


def apply_owner(received, own_blocks):
    slots = received.shape[0]
    classes, fields, levels = own_blocks.shape[0], own_blocks.shape[1], own_blocks.shape[2]
    return pl.pallas_call(
        owner_kernel,
        out_shape=jax.ShapeDtypeStruct((slots, fields * levels), jnp.bfloat16),
        in_specs=[pl.BlockSpec(memory_space=pltpu.VMEM)] * 2,
        out_specs=pl.BlockSpec(memory_space=pltpu.VMEM),
        cost_estimate=pl.CostEstimate(
            flops=2 * slots * classes * fields * levels * levels,
            transcendentals=0,
            bytes_accessed=2 * (received.size + own_blocks.size + slots * fields * levels),
        ),
    )(
        pltpu.with_memory_space_constraint(received, pltpu.MemorySpace.VMEM),
        pltpu.with_memory_space_constraint(own_blocks, pltpu.MemorySpace.VMEM),
    )


def per_device(air_state, owner_map, cost_class, connectivity, inverse_blocks):
    groups = lax.axis_size("row")
    local_count, feat = air_state.shape
    levels = inverse_blocks.shape[-1]
    classes = inverse_blocks.shape[1]
    fields = feat // levels
    capacity = 2 * local_count // groups
    slots = groups * capacity

    outgoing, dest = pack_columns(
        air_state, owner_map.reshape(1, local_count), cost_class.reshape(1, local_count), capacity, slots
    )
    pack = (jnp.arange(slots, dtype=jnp.int32)[:, None] == dest).astype(jnp.bfloat16)
    received = lax.all_to_all(
        outgoing.reshape(groups, capacity, feat + 128), "row", split_axis=0, concat_axis=0, tiled=True
    ).reshape(slots, feat + 128)

    halo = local_count // 4
    extended = padded(air_state, "col", halo)
    base = jnp.arange(local_count, dtype=jnp.int32)[:, None] + halo
    cols = jnp.arange(local_count + 2 * halo, dtype=jnp.int32)[None, :]
    counts = jnp.zeros((local_count, local_count + 2 * halo), jnp.float32)
    for partner in range(connectivity.shape[0]):
        counts = counts + (cols == base + connectivity[partner][:, None]).astype(jnp.float32)
    counts = counts - connectivity.shape[0] * (cols == base).astype(jnp.float32)
    band = (viscosity * counts).astype(jnp.bfloat16)
    lap = jnp.dot(band, extended, preferred_element_type=jnp.float32)

    computed = apply_owner(received, inverse_blocks[0])
    returned = lax.all_to_all(
        computed.reshape(groups, capacity, feat), "row", split_axis=0, concat_axis=0, tiled=True
    ).reshape(slots, feat)
    physics = lax.dot_general(
        pack, returned, (((0,), (0,)), ((), ())), preferred_element_type=jnp.float32
    )
    return (physics + lap).astype(jnp.bfloat16)


def solution(mesh):
    return jax.shard_map(
        per_device,
        mesh=mesh,
        in_specs=(
            P(("row", "col"), None),
            P(("row", "col"), None),
            P(("row", "col")),
            P(None, ("row", "col")),
            P(("row", "col"), None, None, None, None),
        ),
        out_specs=P(("row", "col"), None),
        check_vma=False,
    )
```

```python
import jax
import jax.numpy as jnp
from jax import lax
from jax.experimental import pallas as pl
from jax.experimental.pallas import tpu as pltpu
from jax.sharding import PartitionSpec as P

viscosity = 0.25


def padded(cells, axis, width):
    count = lax.axis_size(axis)
    head = cells[:width]
    tail = cells[cells.shape[0] - width:]
    return jnp.concatenate(
        [
            lax.ppermute(tail, axis, [(i, (i + 1) % count) for i in range(count)]),
            cells,
            lax.ppermute(head, axis, [((i + 1) % count, i) for i in range(count)]),
        ],
        axis=0,
    )


def owner_kernel(x_ref, m_ref, o_ref):
    classes, fields, levels = m_ref.shape[0], m_ref.shape[1], m_ref.shape[2]
    feat = fields * levels
    labels = x_ref[:, feat:feat + 1].astype(jnp.float32)
    for f in range(fields):
        xf = x_ref[:, f * levels:(f + 1) * levels]
        acc = None
        for c in range(classes):
            r = lax.dot_general(
                xf, m_ref[c, f], (((1,), (1,)), ((), ())), preferred_element_type=jnp.float32
            )
            acc = r if acc is None else jnp.where(labels == c, r, acc)
        o_ref[:, f * levels:(f + 1) * levels] = acc.astype(o_ref.dtype)


def apply_owner(received, own_blocks):
    slots = received.shape[0]
    classes, fields, levels = own_blocks.shape[0], own_blocks.shape[1], own_blocks.shape[2]
    return pl.pallas_call(
        owner_kernel,
        out_shape=jax.ShapeDtypeStruct((slots, fields * levels), jnp.bfloat16),
        in_specs=[pl.BlockSpec(memory_space=pltpu.VMEM)] * 2,
        out_specs=pl.BlockSpec(memory_space=pltpu.VMEM),
        cost_estimate=pl.CostEstimate(
            flops=2 * slots * classes * fields * levels * levels,
            transcendentals=0,
            bytes_accessed=2 * (received.size + own_blocks.size + slots * fields * levels),
        ),
    )(
        pltpu.with_memory_space_constraint(received, pltpu.MemorySpace.VMEM),
        pltpu.with_memory_space_constraint(own_blocks, pltpu.MemorySpace.VMEM),
    )


def per_device(air_state, owner_map, cost_class, connectivity, inverse_blocks):
    groups = lax.axis_size("row")
    local_count, feat = air_state.shape
    levels = inverse_blocks.shape[-1]
    classes = inverse_blocks.shape[1]
    fields = feat // levels
    capacity = 2 * local_count // groups
    slots = groups * capacity

    combined = owner_map[:, 0] * classes + cost_class
    targets = combined // classes
    column_class = combined - targets * classes
    hits = (targets[:, None] == jnp.arange(groups, dtype=jnp.int32)[None, :]).astype(jnp.int32)
    slot_index = jnp.sum((jnp.cumsum(hits, axis=0) - 1) * hits, axis=1)
    dest = targets * capacity + slot_index
    pack = (jnp.arange(slots, dtype=jnp.int32)[:, None] == dest[None, :]).astype(jnp.bfloat16)

    label_lanes = jnp.broadcast_to(column_class.astype(jnp.bfloat16)[:, None], (local_count, 128))
    air_ext = jnp.concatenate([air_state, label_lanes], axis=1)
    outgoing = jnp.dot(pack, air_ext, preferred_element_type=jnp.float32).astype(jnp.bfloat16)
    received = lax.all_to_all(
        outgoing.reshape(groups, capacity, feat + 128), "row", split_axis=0, concat_axis=0, tiled=True
    ).reshape(slots, feat + 128)

    halo = local_count // 4
    extended = padded(air_state, "col", halo)
    base = jnp.arange(local_count, dtype=jnp.int32)[:, None] + halo
    cols = jnp.arange(local_count + 2 * halo, dtype=jnp.int32)[None, :]
    counts = jnp.zeros((local_count, local_count + 2 * halo), jnp.float32)
    for partner in range(connectivity.shape[0]):
        counts = counts + (cols == base + connectivity[partner][:, None]).astype(jnp.float32)
    counts = counts - connectivity.shape[0] * (cols == base).astype(jnp.float32)
    band = (viscosity * counts).astype(jnp.bfloat16)
    lap = jnp.dot(band, extended, preferred_element_type=jnp.float32)

    computed = apply_owner(received, inverse_blocks[0])
    returned = lax.all_to_all(
        computed.reshape(groups, capacity, feat), "row", split_axis=0, concat_axis=0, tiled=True
    ).reshape(slots, feat)
    physics = lax.dot_general(
        pack, returned, (((0,), (0,)), ((), ())), preferred_element_type=jnp.float32
    )
    return (physics + lap).astype(jnp.bfloat16)


def solution(mesh):
    return jax.shard_map(
        per_device,
        mesh=mesh,
        in_specs=(
            P(("row", "col"), None),
            P(("row", "col"), None),
            P(("row", "col")),
            P(None, ("row", "col")),
            P(("row", "col"), None, None, None, None),
        ),
        out_specs=P(("row", "col"), None),
        check_vma=False,
    )
```
